512 devices in a mesh: rep: 32 (over z_hi, x, core), exp: 16 (over y, z_lo).
Axes of the slice: x: 4, y: 8, z: 8 (z_hi: 4, z_lo: 2; z = z_hi * 2 + z_lo), core: 2. Of those that a mesh axis runs over, the one named last changes fastest.
Arguments:
- tokens: bfloat16 [65536, 2048], P(('rep', 'exp')), may hold values from -6 to 6
- expert_ids: int32 [65536, 8], P(('rep', 'exp')), may hold values from 0 to 15, all different within a row; in each aligned block of 128 rows (0 to 127, 128 to 255, ...) at most 72 rows name the same one
- route_weights: float32 [65536, 8], P(('rep', 'exp')), may hold values from 0.05 to 1
- placement_map: int32 [16], replicated, may hold values from 0 to 15, each once
- w_gate: bfloat16 [16, 2048, 384], P('exp', 'rep'), may hold values from -0.125 to 0.125
- w_up: bfloat16 [16, 2048, 384], P('exp', 'rep'), may hold values from -0.125 to 0.125
- down_rows: bfloat16 [16, 2048, 384], P('exp', 'rep'), may hold values from -0.3125 to 0.3125
Outputs:
- mixed: bfloat16 [65536, 2048], P(('rep', 'exp'))
The draws below stay inside these ranges and needn't reach their ends.
Inputs may be any that keep to these rules, and one draw needn't show every extreme that they name: `expert_ids`: each row names 8 different experts. Within each device's aligned block of 128 rows no expert is named by more than 72 rows, a bound that some block reaches. `placement_map`: A permutation: every storage index is used once.
All inputs are finite; a program needn't handle non-finite values.
Results may differ from the reference program's by a relative error of at most 0.0057.
Values may be sent and summed in bfloat16 or wider, within the bound.
No kernel may reach another device: no remote copies, remote signals or barrier semaphores. Data moves between devices by JAX's collectives and lax.ppermute only.
A program may use at most 64 MiB of HBM per device.

```python
import math
import jax
import jax.numpy as jnp
import numpy as np
from jax import lax

D = 2048
HWIN = 384
TOPK = 8
EXPERTS = 16
TOK_DEV = 128
CAP = 72
TOKENS = 65536


def block_levels(own_key, dims, split, least, high):
    factor_of = 1.0
    for dim, blocks in split:
        steps = jax.random.uniform(jax.random.fold_in(jax.random.fold_in(own_key, 6), dim), (blocks,), jnp.float32, least / len(split), high / len(split))
        factor_of = factor_of * jnp.repeat(jnp.exp(steps), dims[dim] // blocks).reshape((-1,) + (1,) * (len(dims) - 1 - dim))
    return factor_of


def assign_block(rng, own, number, rows, number_of, top, reach, skew):
    sequence = jax.random.permutation(rng, number_of)
    packed, usual = load_shares(number_of, rows * top, reach, skew, True), load_shares(number_of, rows * top, reach, skew, False)
    places = jnp.arange(number_of)

    def named(lengths, rotation):
        used = int((lengths > 0).sum())
        fixed = max(1, used // 4)
        moved = fixed + (places - fixed + rotation * (used - fixed)) % max(1, number_of - fixed)
        return jnp.zeros((number_of,), jnp.int32).at[sequence[jnp.where(places < fixed, places, moved)]].set(jnp.asarray(lengths, jnp.int32))

    lengths = jnp.where(number % 4 == 0, named(packed, number // 4), named(usual, number - number // 4 - 1))
    mixed = jax.random.permutation(jax.random.fold_in(own, 3), number_of)
    source_of, receiver = mixed[0:number_of // 2 * 2:2], mixed[1:number_of // 2 * 2:2]
    margin = jnp.minimum(lengths[source_of] - 1, reach - lengths[receiver]) // 2
    margin = jnp.where((source_of == sequence[0]) | (receiver == sequence[0]) | (lengths[receiver] == 0), 0, jnp.maximum(margin, 0))
    moved = jax.random.randint(jax.random.fold_in(own, 4), (number_of // 2,), 0, 1 << 20) % (margin + 1)
    lengths = lengths.at[source_of].add(-moved).at[receiver].add(moved)
    members = jnp.searchsorted(jnp.cumsum(lengths), jnp.arange(rows * top), side="right").astype(jnp.int32)
    grid = members.reshape(top, rows).T
    grid = grid[jax.random.permutation(jax.random.fold_in(own, 1), rows)]
    rotation = jax.random.randint(jax.random.fold_in(own, 2), (rows, 1), 0, top)
    return jnp.take_along_axis(grid, (jnp.arange(top)[None, :] + rotation) % top, axis=1)


def load_shares(number_of, total, reach, slope, full):
    loads = [(1 << 20) // math.isqrt(rank ** slope) + 1 for rank in range(1, number_of + 1)]
    largest = reach if full else min(reach, max(-(-total // number_of), total * loads[0] // sum(loads)))
    least = 1 if total - largest >= number_of - 1 else 0
    counts, rest = [largest] + [least] * (number_of - 1), total - largest - least * (number_of - 1)
    while rest > 0:
        free = [i for i in range(1, number_of) if counts[i] < largest] or [i for i in range(1, number_of) if counts[i] < reach]
        mass, budget = sum([loads[i] for i in free]), rest
        for i in free:
            addition = min(reach - counts[i], max(1, budget * loads[i] // mass), rest)
            counts[i] = counts[i] + addition
            rest = rest - addition
    return np.array(counts)


def scatter_about(own_key, shape, width, most, cuts=(), held_as=jnp.bfloat16):
    values = jax.random.normal(own_key, shape, jnp.float32) * width
    if len(cuts) > 0:
        values = block_levels(own_key, shape, cuts, -0.22, 0.18) * values
    return jnp.clip(values, min=-most, max=most).astype(held_as)


def setup_inputs(seed: int = 0) -> dict:
    seeds = jax.random.split(jax.random.key(seed), 8)
    tokens = scatter_about(seeds[0], (TOKENS, D), 1.0, 6.0, ((0, 512),))
    expert_ids_keys = jax.random.split(jax.random.fold_in(seeds[1], 1), TOKENS // TOK_DEV)
    expert_ids_turns = jax.random.permutation(jax.random.fold_in(seeds[1], 3), TOKENS // TOK_DEV)
    expert_ids = jax.vmap(lambda own, number: assign_block(jax.random.fold_in(seeds[1], 2), own, number, TOK_DEV, EXPERTS, TOPK, CAP, 1))(expert_ids_keys, expert_ids_turns).reshape((TOKENS, TOPK))
    route_weights = jnp.clip(jnp.exp(math.log(1.0) - 2.9957323 * jax.random.uniform(seeds[2], (TOKENS, TOPK), jnp.float32) ** block_levels(seeds[2], (TOKENS, TOPK), ((0, 512),), -0.2, 0.2)), 0.05, 1.0)
    placement_map = jax.random.permutation(seeds[3], EXPERTS).astype(jnp.int32)
    w_gate = scatter_about(seeds[4], (EXPERTS, D, HWIN), D ** -0.5, 0.125, ((0, 16), (1, 32)))
    w_up = scatter_about(seeds[5], (EXPERTS, D, HWIN), D ** -0.5, 0.125, ((0, 16), (1, 32)))
    down_rows = scatter_about(seeds[6], (EXPERTS, D, HWIN), HWIN ** -0.5, 0.3125, ((0, 16), (1, 32)))
    return {"tokens": tokens, "expert_ids": expert_ids, "route_weights": route_weights, "placement_map": placement_map, "w_gate": w_gate, "w_up": w_up, "down_rows": down_rows}


def reference(tokens, expert_ids, route_weights, placement_map, w_gate, w_up, down_rows):
    total_rows = tokens.shape[0]
    blocks = total_rows // TOK_DEV
    block_rows = TOK_DEV * TOPK
    slot_ids = placement_map[expert_ids].astype(jnp.int32).reshape(blocks, block_rows)
    weight_rows = route_weights.reshape(blocks, block_rows)
    row_numbers = jnp.arange(block_rows, dtype=jnp.int32)
    row_base = (jnp.arange(blocks, dtype=jnp.int32) * TOK_DEV)[:, None]

    def placed(routed):
        position = jnp.cumsum(routed) - 1
        target = jnp.where(routed == 1, position, CAP).astype(jnp.int32)
        slot_index = jnp.zeros((CAP + 1,), jnp.int32).at[target].set(row_numbers)
        live_mask = jnp.zeros((CAP + 1,), jnp.int32).at[target].set(1)
        return slot_index[:CAP], live_mask[:CAP]

    def expert_step(combined, slot_number):
        routed = (slot_ids == slot_number).astype(jnp.int32)
        slot_index, live_mask = jax.vmap(placed)(routed)
        tok_index = (row_base + slot_index // TOPK).reshape(-1).astype(jnp.int32)
        share_weight = jnp.take_along_axis(weight_rows, slot_index, axis=1) * live_mask.astype(weight_rows.dtype)
        gathered = tokens[tok_index]
        gate_value = jnp.dot(gathered, w_gate[slot_number], preferred_element_type=jnp.float32)
        up_value = jnp.dot(gathered, w_up[slot_number], preferred_element_type=jnp.float32)
        hidden = (jax.nn.silu(gate_value) * up_value).astype(jnp.bfloat16)
        result = jnp.dot(hidden, down_rows[slot_number].T, preferred_element_type=jnp.float32).astype(jnp.bfloat16)
        combined = combined.at[tok_index].add(share_weight.reshape(-1, 1) * result.astype(jnp.float32))
        return combined, None

    start = jnp.zeros((total_rows, D), jnp.float32)
    combined, unused = lax.scan(expert_step, start, jnp.arange(EXPERTS, dtype=jnp.int32))
    return combined.astype(jnp.bfloat16)
```

```python
import jax
import jax.numpy as jnp
from jax import lax
from jax.sharding import PartitionSpec as P

CAP = 72


def apply_experts(received, weights):
    sources, local_count, capacity, model_width = received.shape
    row_block = received[:, 0].reshape(-1, model_width)
    gate_value = jnp.dot(row_block, weights[0, 0], preferred_element_type=jnp.float32)
    up_value = jnp.dot(row_block, weights[1, 0], preferred_element_type=jnp.float32)
    hidden = (jax.nn.silu(gate_value) * up_value).astype(jnp.bfloat16)
    result = lax.dot_general(
        hidden, weights[2, 0], (((1,), (1,)), ((), ())), preferred_element_type=jnp.float32
    )
    results = [result.astype(jnp.bfloat16).reshape(sources, capacity, model_width)]
    return jnp.stack(results, axis=1)


def on_device(tokens, expert_ids, route_weights, placement_map, w_gate, w_up, down_rows):
    tok_rows, top_count = expert_ids.shape
    experts = placement_map.shape[0]
    local_experts = w_gate.shape[0]
    model_width = tokens.shape[1]
    groups = lax.axis_size("exp")
    slots_total = experts * CAP
    expert_range = jnp.arange(experts, dtype=jnp.int32)
    slot_ids = jnp.sum(jnp.where(expert_ids[:, :, None] == expert_range, placement_map, 0), axis=2)
    slot_hot = slot_ids[:, :, None] == expert_range
    token_hot = jnp.sum(slot_hot.astype(jnp.float32), axis=1).astype(jnp.bfloat16)
    row_range = jnp.arange(tok_rows, dtype=jnp.int32)
    earlier = (row_range[None, :] < row_range[:, None]).astype(jnp.bfloat16)
    before = jnp.dot(earlier, token_hot, preferred_element_type=jnp.float32)
    position = jnp.sum(jnp.where(slot_hot, before[:, None, :], 0.0), axis=2).astype(jnp.int32)
    target = slot_ids * CAP + position
    slot_range = jnp.arange(slots_total, dtype=jnp.int32)
    hits = target[:, :, None] == slot_range
    scatter = jnp.sum(hits.astype(jnp.float32), axis=1).astype(jnp.bfloat16)
    outgoing = lax.dot_general(
        scatter, tokens, (((0,), (0,)), ((), ())), preferred_element_type=jnp.float32
    ).astype(jnp.bfloat16)
    outgoing = outgoing.reshape(groups, local_experts, CAP, model_width)
    stacked = jnp.stack([w_gate, w_up, down_rows])
    stacked = lax.all_gather(stacked, "rep", axis=2, tiled=True)
    received = lax.all_to_all(outgoing, "exp", split_axis=0, concat_axis=0, tiled=True)
    returned = lax.all_to_all(
        apply_experts(received, stacked), "exp", split_axis=0, concat_axis=0, tiled=True
    )
    returned = returned.reshape(slots_total, model_width)
    combine = jnp.sum(jnp.where(hits, route_weights[:, :, None], 0.0), axis=1)
    combine_hi = combine.astype(jnp.bfloat16)
    combine_lo = (combine - combine_hi.astype(jnp.float32)).astype(jnp.bfloat16)
    mixed = jnp.dot(combine_hi, returned, preferred_element_type=jnp.float32)
    mixed = mixed + jnp.dot(combine_lo, returned, preferred_element_type=jnp.float32)
    return mixed.astype(jnp.bfloat16)


def solution(mesh):
    return jax.shard_map(
        on_device,
        mesh=mesh,
        in_specs=(
            P(("rep", "exp"), None),
            P(("rep", "exp"), None),
            P(("rep", "exp"), None),
            P(),
            P("exp", "rep", None),
            P("exp", "rep", None),
            P("exp", "rep", None),
        ),
        out_specs=P(("rep", "exp"), None),
        check_vma=False,
    )
```

```python
import jax
import jax.numpy as jnp
from jax import lax
from jax.sharding import Mesh, PartitionSpec as P

CAP = 72


def apply_experts(received, weights):
    sources, local_count, capacity, model_width = received.shape
    row_block = received[:, 0].reshape(-1, model_width)
    gate_value = jnp.dot(row_block, weights[0, 0], preferred_element_type=jnp.float32)
    up_value = jnp.dot(row_block, weights[1, 0], preferred_element_type=jnp.float32)
    hidden = (jax.nn.silu(gate_value) * up_value).astype(jnp.bfloat16)
    result = lax.dot_general(
        hidden, weights[2, 0], (((1,), (1,)), ((), ())), preferred_element_type=jnp.float32
    )
    results = [result.astype(jnp.bfloat16).reshape(sources, capacity, model_width)]
    return jnp.stack(results, axis=1)


def on_device(tokens, expert_ids, route_weights, placement_map, w_gate, w_up, down_rows):
    tok_rows, top_count = expert_ids.shape
    experts = placement_map.shape[0]
    local_experts = w_gate.shape[0]
    model_width = tokens.shape[1]
    groups = experts
    slots_total = experts * CAP
    expert_range = jnp.arange(experts, dtype=jnp.int32)
    slot_ids = jnp.sum(jnp.where(expert_ids[:, :, None] == expert_range, placement_map, 0), axis=2)
    slot_hot = slot_ids[:, :, None] == expert_range
    token_hot = jnp.sum(slot_hot.astype(jnp.float32), axis=1).astype(jnp.bfloat16)
    row_range = jnp.arange(tok_rows, dtype=jnp.int32)
    earlier = (row_range[None, :] < row_range[:, None]).astype(jnp.bfloat16)
    before = jnp.dot(earlier, token_hot, preferred_element_type=jnp.float32)
    position = jnp.sum(jnp.where(slot_hot, before[:, None, :], 0.0), axis=2).astype(jnp.int32)
    target = slot_ids * CAP + position
    slot_range = jnp.arange(slots_total, dtype=jnp.int32)
    hits = target[:, :, None] == slot_range
    scatter = jnp.sum(hits.astype(jnp.float32), axis=1).astype(jnp.bfloat16)
    outgoing = lax.dot_general(
        scatter, tokens, (((0,), (0,)), ((), ())), preferred_element_type=jnp.float32
    ).astype(jnp.bfloat16)
    outgoing = outgoing.reshape(groups, local_experts, CAP, model_width)
    stacked = jnp.stack([w_gate, w_up, down_rows])
    stacked = lax.all_gather(stacked, "y", axis=1, tiled=True)
    stacked = lax.all_to_all(stacked, ("x", "c"), split_axis=1, concat_axis=1, tiled=True)
    stacked = stacked.reshape(3, 1, -1, stacked.shape[-1])
    stacked = lax.all_gather(stacked, "zh", axis=2, tiled=True)
    team = ("x", "c", "zl")
    received = lax.all_to_all(outgoing, team, split_axis=0, concat_axis=0, tiled=True)
    returned = lax.all_to_all(
        apply_experts(received, stacked), team, split_axis=0, concat_axis=0, tiled=True
    )
    returned = returned.reshape(slots_total, model_width)
    combine = jnp.sum(jnp.where(hits, route_weights[:, :, None], 0.0), axis=1)
    combine_hi = combine.astype(jnp.bfloat16)
    combine_lo = (combine - combine_hi.astype(jnp.float32)).astype(jnp.bfloat16)
    mixed = jnp.dot(combine_hi, returned, preferred_element_type=jnp.float32)
    mixed = mixed + jnp.dot(combine_lo, returned, preferred_element_type=jnp.float32)
    return mixed.astype(jnp.bfloat16)


def solution(mesh):
    fine = Mesh(mesh.devices.reshape(4, 4, 2, 8, 2), ("zh", "x", "c", "y", "zl"))
    rows = ("zh", "x", "c", "y", "zl")
    weight_spec = P(("y", "zl"), ("zh", "x", "c"), None)
    return jax.shard_map(
        on_device,
        mesh=fine,
        in_specs=(
            P(rows, None),
            P(rows, None),
            P(rows, None),
            P(),
            weight_spec,
            weight_spec,
            weight_spec,
        ),
        out_specs=P(rows, None),
        check_vma=False,
    )
```

```python
import jax
import jax.numpy as jnp
from jax import lax
from jax.sharding import PartitionSpec as P

CAP = 72


def apply_experts(received, weights):
    sources, local_count, capacity, model_width = received.shape
    row_block = received[:, 0].reshape(-1, model_width)
    gate_value = jnp.dot(row_block, weights[0][0], preferred_element_type=jnp.float32)
    up_value = jnp.dot(row_block, weights[1][0], preferred_element_type=jnp.float32)
    hidden = (jax.nn.silu(gate_value) * up_value).astype(jnp.bfloat16)
    result = lax.dot_general(
        hidden, weights[2][0], (((1,), (1,)), ((), ())), preferred_element_type=jnp.float32
    )
    results = [result.astype(jnp.bfloat16).reshape(sources, capacity, model_width)]
    return jnp.stack(results, axis=1)


def on_device(tokens, expert_ids, route_weights, placement_map, w_gate, w_up, down_rows):
    tok_rows, top_count = expert_ids.shape
    experts = placement_map.shape[0]
    local_experts = w_gate.shape[0]
    model_width = tokens.shape[1]
    groups = lax.axis_size("exp")
    slots_total = experts * CAP
    expert_range = jnp.arange(experts, dtype=jnp.int32)
    slot_ids = jnp.sum(jnp.where(expert_ids[:, :, None] == expert_range, placement_map, 0), axis=2)
    slot_hot = slot_ids[:, :, None] == expert_range
    token_hot = jnp.sum(slot_hot.astype(jnp.float32), axis=1)
    row_range = jnp.arange(tok_rows, dtype=jnp.int32)
    earlier = (row_range[None, :] < row_range[:, None]).astype(jnp.bfloat16)
    before = jnp.dot(earlier, token_hot.astype(jnp.bfloat16), preferred_element_type=jnp.float32)
    picked_weight = jnp.sum(jnp.where(slot_hot, route_weights[:, :, None], 0.0), axis=1)
    cap_range = jnp.arange(CAP, dtype=jnp.float32)
    placed = (before[:, :, None] == cap_range) & (token_hot[:, :, None] > 0.5)
    scatter = placed.astype(jnp.bfloat16).reshape(tok_rows, slots_total)
    outgoing = lax.dot_general(
        scatter, tokens, (((0,), (0,)), ((), ())), preferred_element_type=jnp.float32
    ).astype(jnp.bfloat16)
    outgoing = outgoing.reshape(groups, local_experts, CAP, model_width)
    gathered = [lax.all_gather(w, "rep", axis=1, tiled=True) for w in (w_gate, w_up, down_rows)]
    received = lax.all_to_all(outgoing, "exp", split_axis=0, concat_axis=0, tiled=True)
    returned = lax.all_to_all(
        apply_experts(received, gathered), "exp", split_axis=0, concat_axis=0, tiled=True
    )
    returned = returned.reshape(slots_total, model_width)
    combine = jnp.where(placed, picked_weight[:, :, None], 0.0).reshape(tok_rows, slots_total)
    combine_hi = combine.astype(jnp.bfloat16)
    combine_lo = (combine - combine_hi.astype(jnp.float32)).astype(jnp.bfloat16)
    mixed = jnp.dot(combine_hi, returned, preferred_element_type=jnp.float32)
    mixed = mixed + jnp.dot(combine_lo, returned, preferred_element_type=jnp.float32)
    return mixed.astype(jnp.bfloat16)


def solution(mesh):
    return jax.shard_map(
        on_device,
        mesh=mesh,
        in_specs=(
            P(("rep", "exp"), None),
            P(("rep", "exp"), None),
            P(("rep", "exp"), None),
            P(),
            P("exp", "rep", None),
            P("exp", "rep", None),
            P("exp", "rep", None),
        ),
        out_specs=P(("rep", "exp"), None),
        check_vma=False,
    )
```

```python
import jax
import jax.numpy as jnp
from jax import lax
from jax.sharding import PartitionSpec as P

CAP = 72


def apply_experts(received, weights):
    sources, local_count, capacity, model_width = received.shape
    hidden_width = weights.shape[-1]
    row_block = received[:, 0].reshape(-1, model_width)
    gate_up = jnp.concatenate([weights[0, 0], weights[1, 0]], axis=1)
    both = jnp.dot(row_block, gate_up, preferred_element_type=jnp.float32)
    gate_value, up_value = both[:, :hidden_width], both[:, hidden_width:]
    hidden = (jax.nn.silu(gate_value) * up_value).astype(jnp.bfloat16)
    hidden = lax.optimization_barrier(hidden)
    result = lax.dot_general(
        hidden, weights[2, 0], (((1,), (1,)), ((), ())), preferred_element_type=jnp.float32
    )
    results = [result.astype(jnp.bfloat16).reshape(sources, capacity, model_width)]
    return jnp.stack(results, axis=1)


def on_device(tokens, expert_ids, route_weights, placement_map, w_gate, w_up, down_rows):
    tok_rows, top_count = expert_ids.shape
    experts = placement_map.shape[0]
    local_experts = w_gate.shape[0]
    model_width = tokens.shape[1]
    groups = lax.axis_size("exp")
    slots_total = experts * CAP
    expert_range = jnp.arange(experts, dtype=jnp.int32)
    slot_ids = jnp.sum(jnp.where(expert_ids[:, :, None] == expert_range, placement_map, 0), axis=2)
    slot_hot = slot_ids[:, :, None] == expert_range
    token_hot = jnp.sum(slot_hot.astype(jnp.float32), axis=1).astype(jnp.bfloat16)
    row_range = jnp.arange(tok_rows, dtype=jnp.int32)
    earlier = (row_range[None, :] < row_range[:, None]).astype(jnp.bfloat16)
    before = jnp.dot(earlier, token_hot, preferred_element_type=jnp.float32)
    position = jnp.sum(jnp.where(slot_hot, before[:, None, :], 0.0), axis=2).astype(jnp.int32)
    target = slot_ids * CAP + position
    slot_range = jnp.arange(slots_total, dtype=jnp.int32)
    hits = target[:, :, None] == slot_range
    scatter = jnp.sum(hits.astype(jnp.float32), axis=1).astype(jnp.bfloat16)
    outgoing = lax.dot_general(
        scatter, tokens, (((0,), (0,)), ((), ())), preferred_element_type=jnp.float32
    ).astype(jnp.bfloat16)
    outgoing = outgoing.reshape(groups, local_experts, CAP, model_width)
    stacked = jnp.stack([w_gate, w_up, down_rows])
    stacked = lax.all_gather(stacked, "rep", axis=2, tiled=True)
    received = lax.all_to_all(outgoing, "exp", split_axis=0, concat_axis=0, tiled=True)
    returned = lax.all_to_all(
        apply_experts(received, stacked), "exp", split_axis=0, concat_axis=0, tiled=True
    )
    returned = returned.reshape(slots_total, model_width)
    combine = jnp.sum(jnp.where(hits, route_weights[:, :, None], 0.0), axis=1)
    combine_hi = combine.astype(jnp.bfloat16)
    combine_lo = (combine - combine_hi.astype(jnp.float32)).astype(jnp.bfloat16)
    mixed = jnp.dot(combine_hi, returned, preferred_element_type=jnp.float32)
    mixed = mixed + jnp.dot(combine_lo, returned, preferred_element_type=jnp.float32)
    return mixed.astype(jnp.bfloat16)


def solution(mesh):
    return jax.shard_map(
        on_device,
        mesh=mesh,
        in_specs=(
            P(("rep", "exp"), None),
            P(("rep", "exp"), None),
            P(("rep", "exp"), None),
            P(),
            P("exp", "rep", None),
            P("exp", "rep", None),
            P("exp", "rep", None),
        ),
        out_specs=P(("rep", "exp"), None),
        check_vma=False,
    )
```

```python
import jax
import jax.numpy as jnp
from jax import lax
from jax.sharding import PartitionSpec as P

CAP = 72


def apply_experts(received, weights):
    sources, local_count, capacity, model_width = received.shape
    row_block = received[:, 0].reshape(-1, model_width)
    gate_value = jnp.dot(row_block, weights[0, 0], preferred_element_type=jnp.float32)
    up_value = jnp.dot(row_block, weights[1, 0], preferred_element_type=jnp.float32)
    hidden = (jax.nn.silu(gate_value) * up_value).astype(jnp.bfloat16)
    result = lax.dot_general(
        hidden, weights[2, 0], (((1,), (1,)), ((), ())), preferred_element_type=jnp.float32
    )
    results = [result.astype(jnp.bfloat16).reshape(sources, capacity, model_width)]
    return jnp.stack(results, axis=1)


def on_device(tokens, expert_ids, route_weights, placement_map, w_gate, w_up, down_rows):
    tok_rows, top_count = expert_ids.shape
    experts = placement_map.shape[0]
    local_experts = w_gate.shape[0]
    model_width = tokens.shape[1]
    groups = lax.axis_size("exp")
    slots_total = experts * CAP
    expert_range = jnp.arange(experts, dtype=jnp.int32)
    slot_ids = jnp.sum(jnp.where(expert_ids[:, :, None] == expert_range, placement_map, 0), axis=2)
    slot_hot = slot_ids[:, :, None] == expert_range
    token_hot = jnp.sum(slot_hot.astype(jnp.float32), axis=1).astype(jnp.bfloat16)
    row_range = jnp.arange(tok_rows, dtype=jnp.int32)
    earlier = (row_range[None, :] < row_range[:, None]).astype(jnp.bfloat16)
    before = jnp.dot(earlier, token_hot, preferred_element_type=jnp.float32)
    position = jnp.sum(jnp.where(slot_hot, before[:, None, :], 0.0), axis=2).astype(jnp.int32)
    target = slot_ids * CAP + position
    slot_range = jnp.arange(slots_total, dtype=jnp.int32)
    hits = target[:, :, None] == slot_range
    scatter = jnp.sum(hits.astype(jnp.float32), axis=1).astype(jnp.bfloat16)
    outgoing = lax.dot_general(
        scatter, tokens, (((0,), (0,)), ((), ())), preferred_element_type=jnp.float32
    ).astype(jnp.bfloat16)
    outgoing = outgoing.reshape(groups, local_experts, CAP, model_width)
    stacked = jnp.stack([w_gate, w_up, down_rows])
    copies = lax.axis_size("rep")
    me = lax.axis_index("rep")
    pieces = [stacked]
    for shift in range(1, copies):
        pairs = [(i, (i + shift) % copies) for i in range(copies)]
        pieces.append(lax.ppermute(stacked, "rep", pairs))
    ordered = jnp.stack(pieces)
    order = (me - jnp.arange(copies, dtype=jnp.int32)) % copies
    inverse = jnp.zeros((copies,), jnp.int32).at[order].set(jnp.arange(copies, dtype=jnp.int32))
    ordered = jnp.take(ordered, inverse, axis=0)
    stacked = jnp.moveaxis(ordered, 0, 2).reshape(3, 1, -1, stacked.shape[-1])
    received = lax.all_to_all(outgoing, "exp", split_axis=0, concat_axis=0, tiled=True)
    returned = lax.all_to_all(
        apply_experts(received, stacked), "exp", split_axis=0, concat_axis=0, tiled=True
    )
    returned = returned.reshape(slots_total, model_width)
    combine = jnp.sum(jnp.where(hits, route_weights[:, :, None], 0.0), axis=1)
    combine_hi = combine.astype(jnp.bfloat16)
    combine_lo = (combine - combine_hi.astype(jnp.float32)).astype(jnp.bfloat16)
    mixed = jnp.dot(combine_hi, returned, preferred_element_type=jnp.float32)
    mixed = mixed + jnp.dot(combine_lo, returned, preferred_element_type=jnp.float32)
    return mixed.astype(jnp.bfloat16)


def solution(mesh):
    return jax.shard_map(
        on_device,
        mesh=mesh,
        in_specs=(
            P(("rep", "exp"), None),
            P(("rep", "exp"), None),
            P(("rep", "exp"), None),
            P(),
            P("exp", "rep", None),
            P("exp", "rep", None),
            P("exp", "rep", None),
        ),
        out_specs=P(("rep", "exp"), None),
        check_vma=False,
    )
```

```python
import jax
import jax.numpy as jnp
from jax import lax
from jax.sharding import PartitionSpec as P

CAP = 72


def apply_experts(received, weights):
    sources, local_count, capacity, model_width = received.shape
    row_block = received[:, 0].reshape(-1, model_width)
    gate_value = jnp.dot(row_block, weights[0, 0], preferred_element_type=jnp.float32)
    up_value = jnp.dot(row_block, weights[1, 0], preferred_element_type=jnp.float32)
    hidden = (jax.nn.silu(gate_value) * up_value).astype(jnp.bfloat16)
    result = lax.dot_general(
        hidden, weights[2, 0], (((1,), (1,)), ((), ())), preferred_element_type=jnp.float32
    )
    results = [result.astype(jnp.bfloat16).reshape(sources, capacity, model_width)]
    return jnp.stack(results, axis=1)


def on_device(tokens, expert_ids, route_weights, placement_map, w_gate, w_up, down_rows):
    tok_rows, top_count = expert_ids.shape
    experts = placement_map.shape[0]
    local_experts = w_gate.shape[0]
    model_width = tokens.shape[1]
    groups = lax.axis_size("exp")
    slots_total = experts * CAP
    expert_range = jnp.arange(experts, dtype=jnp.int32)
    slot_ids = jnp.sum(jnp.where(expert_ids[:, :, None] == expert_range, placement_map, 0), axis=2)
    slot_hot = slot_ids[:, :, None] == expert_range
    token_hot = jnp.sum(slot_hot.astype(jnp.float32), axis=1).astype(jnp.bfloat16)
    row_range = jnp.arange(tok_rows, dtype=jnp.int32)
    earlier = (row_range[None, :] < row_range[:, None]).astype(jnp.bfloat16)
    before = jnp.dot(earlier, token_hot, preferred_element_type=jnp.float32)
    position = jnp.sum(jnp.where(slot_hot, before[:, None, :], 0.0), axis=2).astype(jnp.int32)
    target = slot_ids * CAP + position
    slot_range = jnp.arange(slots_total, dtype=jnp.int32)
    hits = target.T[:, :, None] == slot_range
    scatter = jnp.sum(hits.astype(jnp.float32), axis=0).astype(jnp.bfloat16)
    outgoing = lax.dot_general(
        scatter, tokens, (((0,), (0,)), ((), ())), preferred_element_type=jnp.float32
    ).astype(jnp.bfloat16)
    outgoing = outgoing.reshape(groups, local_experts, CAP, model_width)
    stacked = jnp.stack([w_gate, w_up, down_rows])
    stacked = lax.all_gather(stacked, "rep", axis=2, tiled=True)
    received = lax.all_to_all(outgoing, "exp", split_axis=0, concat_axis=0, tiled=True)
    returned = lax.all_to_all(
        apply_experts(received, stacked), "exp", split_axis=0, concat_axis=0, tiled=True
    )
    returned = returned.reshape(slots_total, model_width)
    combine = jnp.sum(jnp.where(hits, route_weights.T[:, :, None], 0.0), axis=0)
    combine_hi = combine.astype(jnp.bfloat16)
    combine_lo = (combine - combine_hi.astype(jnp.float32)).astype(jnp.bfloat16)
    mixed = jnp.dot(combine_hi, returned, preferred_element_type=jnp.float32)
    mixed = mixed + jnp.dot(combine_lo, returned, preferred_element_type=jnp.float32)
    return mixed.astype(jnp.bfloat16)


def solution(mesh):
    return jax.shard_map(
        on_device,
        mesh=mesh,
        in_specs=(
            P(("rep", "exp"), None),
            P(("rep", "exp"), None),
            P(("rep", "exp"), None),
            P(),
            P("exp", "rep", None),
            P("exp", "rep", None),
            P("exp", "rep", None),
        ),
        out_specs=P(("rep", "exp"), None),
        check_vma=False,
    )
```

```python
import jax
import jax.numpy as jnp
from jax import lax
from jax.sharding import PartitionSpec as P

CAP = 72


def apply_experts(received, weights):
    sources, local_count, capacity, model_width = received.shape
    row_block = received[:, 0].reshape(-1, model_width)
    gate_value = jnp.dot(row_block, weights[0, 0], preferred_element_type=jnp.float32)
    up_value = jnp.dot(row_block, weights[1, 0], preferred_element_type=jnp.float32)
    hidden = (jax.nn.silu(gate_value) * up_value).astype(jnp.bfloat16)
    hidden = lax.optimization_barrier(hidden)
    result = lax.dot_general(
        hidden, weights[2, 0], (((1,), (1,)), ((), ())), preferred_element_type=jnp.float32
    )
    results = [result.astype(jnp.bfloat16).reshape(sources, capacity, model_width)]
    return jnp.stack(results, axis=1)


def on_device(tokens, expert_ids, route_weights, placement_map, w_gate, w_up, down_rows):
    tok_rows, top_count = expert_ids.shape
    experts = placement_map.shape[0]
    local_experts = w_gate.shape[0]
    model_width = tokens.shape[1]
    groups = lax.axis_size("exp")
    slots_total = experts * CAP
    expert_range = jnp.arange(experts, dtype=jnp.int32)
    slot_ids = jnp.sum(jnp.where(expert_ids[:, :, None] == expert_range, placement_map, 0), axis=2)
    slot_hot = slot_ids[:, :, None] == expert_range
    token_hot = jnp.sum(slot_hot.astype(jnp.float32), axis=1).astype(jnp.bfloat16)
    row_range = jnp.arange(tok_rows, dtype=jnp.int32)
    earlier = (row_range[None, :] < row_range[:, None]).astype(jnp.bfloat16)
    before = jnp.dot(earlier, token_hot, preferred_element_type=jnp.float32)
    position = jnp.sum(jnp.where(slot_hot, before[:, None, :], 0.0), axis=2).astype(jnp.int32)
    target = slot_ids * CAP + position
    slot_range = jnp.arange(slots_total, dtype=jnp.int32)
    hits = target.T[:, :, None] == slot_range
    scatter = jnp.sum(hits.astype(jnp.float32), axis=0).astype(jnp.bfloat16)
    outgoing = lax.dot_general(
        scatter, tokens, (((0,), (0,)), ((), ())), preferred_element_type=jnp.float32
    ).astype(jnp.bfloat16)
    outgoing = outgoing.reshape(groups, local_experts, CAP, model_width)
    stacked = jnp.stack([w_gate, w_up, down_rows])
    stacked = lax.all_gather(stacked, "rep", axis=2, tiled=True)
    received = lax.all_to_all(outgoing, "exp", split_axis=0, concat_axis=0, tiled=True)
    returned = lax.all_to_all(
        apply_experts(received, stacked), "exp", split_axis=0, concat_axis=0, tiled=True
    )
    returned = returned.reshape(slots_total, model_width)
    combine = jnp.sum(jnp.where(hits, route_weights.T[:, :, None], 0.0), axis=0)
    combine_hi = combine.astype(jnp.bfloat16)
    combine_lo = (combine - combine_hi.astype(jnp.float32)).astype(jnp.bfloat16)
    mixed = jnp.dot(combine_hi, returned, preferred_element_type=jnp.float32)
    mixed = mixed + jnp.dot(combine_lo, returned, preferred_element_type=jnp.float32)
    return mixed.astype(jnp.bfloat16)


def solution(mesh):
    return jax.shard_map(
        on_device,
        mesh=mesh,
        in_specs=(
            P(("rep", "exp"), None),
            P(("rep", "exp"), None),
            P(("rep", "exp"), None),
            P(),
            P("exp", "rep", None),
            P("exp", "rep", None),
            P("exp", "rep", None),
        ),
        out_specs=P(("rep", "exp"), None),
        check_vma=False,
    )
```

```python
import jax
import jax.numpy as jnp
from jax import lax
from jax.sharding import PartitionSpec as P

CAP = 72


def apply_experts(received, weights, hidden_width):
    sources, local_count, capacity, model_width = received.shape
    row_block = received[:, 0].reshape(-1, model_width)
    both = jnp.dot(row_block, weights[0, :, : 2 * hidden_width], preferred_element_type=jnp.float32)
    gate_value, up_value = both[:, :hidden_width], both[:, hidden_width:]
    hidden = (jax.nn.silu(gate_value) * up_value).astype(jnp.bfloat16)
    hidden = lax.optimization_barrier(hidden)
    result = lax.dot_general(
        hidden, weights[0, :, 2 * hidden_width :], (((1,), (1,)), ((), ())),
        preferred_element_type=jnp.float32,
    )
    results = [result.astype(jnp.bfloat16).reshape(sources, capacity, model_width)]
    return jnp.stack(results, axis=1)


def on_device(tokens, expert_ids, route_weights, placement_map, w_gate, w_up, down_rows):
    tok_rows, top_count = expert_ids.shape
    experts = placement_map.shape[0]
    local_experts = w_gate.shape[0]
    model_width = tokens.shape[1]
    groups = lax.axis_size("exp")
    slots_total = experts * CAP
    expert_range = jnp.arange(experts, dtype=jnp.int32)
    slot_ids = jnp.sum(jnp.where(expert_ids[:, :, None] == expert_range, placement_map, 0), axis=2)
    slot_hot = slot_ids[:, :, None] == expert_range
    token_hot = jnp.sum(slot_hot.astype(jnp.float32), axis=1).astype(jnp.bfloat16)
    row_range = jnp.arange(tok_rows, dtype=jnp.int32)
    earlier = (row_range[None, :] < row_range[:, None]).astype(jnp.bfloat16)
    before = jnp.dot(earlier, token_hot, preferred_element_type=jnp.float32)
    position = jnp.sum(jnp.where(slot_hot, before[:, None, :], 0.0), axis=2).astype(jnp.int32)
    target = slot_ids * CAP + position
    slot_range = jnp.arange(slots_total, dtype=jnp.int32)
    hits = target.T[:, :, None] == slot_range
    scatter = jnp.sum(hits.astype(jnp.float32), axis=0).astype(jnp.bfloat16)
    outgoing = lax.dot_general(
        scatter, tokens, (((0,), (0,)), ((), ())), preferred_element_type=jnp.float32
    ).astype(jnp.bfloat16)
    outgoing = outgoing.reshape(groups, local_experts, CAP, model_width)
    stacked = jnp.concatenate([w_gate, w_up, down_rows], axis=2)
    stacked = lax.all_gather(stacked, "rep", axis=1, tiled=True)
    received = lax.all_to_all(outgoing, "exp", split_axis=0, concat_axis=0, tiled=True)
    returned = lax.all_to_all(
        apply_experts(received, stacked, w_gate.shape[2]), "exp", split_axis=0, concat_axis=0, tiled=True
    )
    returned = returned.reshape(slots_total, model_width)
    combine = jnp.sum(jnp.where(hits, route_weights.T[:, :, None], 0.0), axis=0)
    combine_hi = combine.astype(jnp.bfloat16)
    combine_lo = (combine - combine_hi.astype(jnp.float32)).astype(jnp.bfloat16)
    mixed = jnp.dot(combine_hi, returned, preferred_element_type=jnp.float32)
    mixed = mixed + jnp.dot(combine_lo, returned, preferred_element_type=jnp.float32)
    return mixed.astype(jnp.bfloat16)


def solution(mesh):
    return jax.shard_map(
        on_device,
        mesh=mesh,
        in_specs=(
            P(("rep", "exp"), None),
            P(("rep", "exp"), None),
            P(("rep", "exp"), None),
            P(),
            P("exp", "rep", None),
            P("exp", "rep", None),
            P("exp", "rep", None),
        ),
        out_specs=P(("rep", "exp"), None),
        check_vma=False,
    )
```

```python
import jax
import jax.numpy as jnp
from jax import lax
from jax.sharding import PartitionSpec as P

CAP = 72


def apply_experts(received, weights):
    sources, local_count, capacity, model_width = received.shape
    row_block = received[:, 0].reshape(-1, model_width)
    gate_value = jnp.dot(row_block, weights[0, 0], preferred_element_type=jnp.float32)
    up_value = jnp.dot(row_block, weights[1, 0], preferred_element_type=jnp.float32)
    gate_value, up_value = lax.optimization_barrier((gate_value, up_value))
    hidden = (jax.nn.silu(gate_value) * up_value).astype(jnp.bfloat16)
    result = lax.dot_general(
        hidden, weights[2, 0], (((1,), (1,)), ((), ())), preferred_element_type=jnp.float32
    )
    results = [result.astype(jnp.bfloat16).reshape(sources, capacity, model_width)]
    return jnp.stack(results, axis=1)


def on_device(tokens, expert_ids, route_weights, placement_map, w_gate, w_up, down_rows):
    tok_rows, top_count = expert_ids.shape
    experts = placement_map.shape[0]
    local_experts = w_gate.shape[0]
    model_width = tokens.shape[1]
    groups = lax.axis_size("exp")
    slots_total = experts * CAP
    expert_range = jnp.arange(experts, dtype=jnp.int32)
    slot_ids = jnp.sum(jnp.where(expert_ids[:, :, None] == expert_range, placement_map, 0), axis=2)
    slot_hot = slot_ids[:, :, None] == expert_range
    token_hot = jnp.sum(slot_hot.astype(jnp.float32), axis=1).astype(jnp.bfloat16)
    row_range = jnp.arange(tok_rows, dtype=jnp.int32)
    earlier = (row_range[None, :] < row_range[:, None]).astype(jnp.bfloat16)
    before = jnp.dot(earlier, token_hot, preferred_element_type=jnp.float32)
    position = jnp.sum(jnp.where(slot_hot, before[:, None, :], 0.0), axis=2).astype(jnp.int32)
    target = slot_ids * CAP + position
    slot_range = jnp.arange(slots_total, dtype=jnp.int32)
    hits = target.T[:, :, None] == slot_range
    scatter = jnp.sum(hits.astype(jnp.float32), axis=0).astype(jnp.bfloat16)
    outgoing = lax.dot_general(
        scatter, tokens, (((0,), (0,)), ((), ())), preferred_element_type=jnp.float32
    ).astype(jnp.bfloat16)
    outgoing = outgoing.reshape(groups, local_experts, CAP, model_width)
    stacked = jnp.stack([w_gate, w_up, down_rows])
    stacked = lax.all_gather(stacked, "rep", axis=2, tiled=True)
    received = lax.all_to_all(outgoing, "exp", split_axis=0, concat_axis=0, tiled=True)
    returned = lax.all_to_all(
        apply_experts(received, stacked), "exp", split_axis=0, concat_axis=0, tiled=True
    )
    returned = returned.reshape(slots_total, model_width)
    combine = jnp.sum(jnp.where(hits, route_weights.T[:, :, None], 0.0), axis=0)
    combine_hi = combine.astype(jnp.bfloat16)
    combine_lo = (combine - combine_hi.astype(jnp.float32)).astype(jnp.bfloat16)
    mixed = jnp.dot(combine_hi, returned, preferred_element_type=jnp.float32)
    mixed = mixed + jnp.dot(combine_lo, returned, preferred_element_type=jnp.float32)
    return mixed.astype(jnp.bfloat16)


def solution(mesh):
    return jax.shard_map(
        on_device,
        mesh=mesh,
        in_specs=(
            P(("rep", "exp"), None),
            P(("rep", "exp"), None),
            P(("rep", "exp"), None),
            P(),
            P("exp", "rep", None),
            P("exp", "rep", None),
            P("exp", "rep", None),
        ),
        out_specs=P(("rep", "exp"), None),
        check_vma=False,
    )
```

```python
import jax
import jax.numpy as jnp
from jax import lax
from jax.experimental import pallas as pl
from jax.sharding import PartitionSpec as P

CAP = 72


def expert_block(x_ref, gate_ref, up_ref, down_ref, out_ref):
    x = x_ref[...]
    gate_value = jnp.dot(x, gate_ref[...], preferred_element_type=jnp.float32)
    up_value = jnp.dot(x, up_ref[...], preferred_element_type=jnp.float32)
    hidden = (gate_value / (1.0 + jnp.exp(-gate_value)) * up_value).astype(jnp.bfloat16)
    result = lax.dot_general(
        hidden, down_ref[...], (((1,), (1,)), ((), ())), preferred_element_type=jnp.float32
    )
    out_ref[...] = result.astype(out_ref.dtype)


def apply_experts(received, weights):
    sources, local_count, capacity, model_width = received.shape
    hidden_width = weights.shape[-1]
    row_block = received[:, 0].reshape(-1, model_width)
    rows = row_block.shape[0]
    block = 128
    weight_spec = pl.BlockSpec((model_width, hidden_width), lambda i: (0, 0))
    result = pl.pallas_call(
        expert_block,
        grid=(rows // block,),
        in_specs=[pl.BlockSpec((block, model_width), lambda i: (i, 0)), weight_spec, weight_spec, weight_spec],
        out_specs=pl.BlockSpec((block, model_width), lambda i: (i, 0)),
        out_shape=jax.ShapeDtypeStruct((rows, model_width), jnp.bfloat16),
    )(row_block, weights[0, 0], weights[1, 0], weights[2, 0])
    results = [result.reshape(sources, capacity, model_width)]
    return jnp.stack(results, axis=1)


def on_device(tokens, expert_ids, route_weights, placement_map, w_gate, w_up, down_rows):
    tok_rows, top_count = expert_ids.shape
    experts = placement_map.shape[0]
    local_experts = w_gate.shape[0]
    model_width = tokens.shape[1]
    groups = lax.axis_size("exp")
    slots_total = experts * CAP
    expert_range = jnp.arange(experts, dtype=jnp.int32)
    slot_ids = jnp.sum(jnp.where(expert_ids[:, :, None] == expert_range, placement_map, 0), axis=2)
    slot_hot = slot_ids[:, :, None] == expert_range
    token_hot = jnp.sum(slot_hot.astype(jnp.float32), axis=1).astype(jnp.bfloat16)
    row_range = jnp.arange(tok_rows, dtype=jnp.int32)
    earlier = (row_range[None, :] < row_range[:, None]).astype(jnp.bfloat16)
    before = jnp.dot(earlier, token_hot, preferred_element_type=jnp.float32)
    position = jnp.sum(jnp.where(slot_hot, before[:, None, :], 0.0), axis=2).astype(jnp.int32)
    target = slot_ids * CAP + position
    slot_range = jnp.arange(slots_total, dtype=jnp.int32)
    hits = target.T[:, :, None] == slot_range
    scatter = jnp.sum(hits.astype(jnp.float32), axis=0).astype(jnp.bfloat16)
    outgoing = lax.dot_general(
        scatter, tokens, (((0,), (0,)), ((), ())), preferred_element_type=jnp.float32
    ).astype(jnp.bfloat16)
    outgoing = outgoing.reshape(groups, local_experts, CAP, model_width)
    stacked = jnp.stack([w_gate, w_up, down_rows])
    stacked = lax.all_gather(stacked, "rep", axis=2, tiled=True)
    received = lax.all_to_all(outgoing, "exp", split_axis=0, concat_axis=0, tiled=True)
    returned = lax.all_to_all(
        apply_experts(received, stacked), "exp", split_axis=0, concat_axis=0, tiled=True
    )
    returned = returned.reshape(slots_total, model_width)
    combine = jnp.sum(jnp.where(hits, route_weights.T[:, :, None], 0.0), axis=0)
    combine_hi = combine.astype(jnp.bfloat16)
    combine_lo = (combine - combine_hi.astype(jnp.float32)).astype(jnp.bfloat16)
    mixed = jnp.dot(combine_hi, returned, preferred_element_type=jnp.float32)
    mixed = mixed + jnp.dot(combine_lo, returned, preferred_element_type=jnp.float32)
    return mixed.astype(jnp.bfloat16)


def solution(mesh):
    return jax.shard_map(
        on_device,
        mesh=mesh,
        in_specs=(
            P(("rep", "exp"), None),
            P(("rep", "exp"), None),
            P(("rep", "exp"), None),
            P(),
            P("exp", "rep", None),
            P("exp", "rep", None),
            P("exp", "rep", None),
        ),
        out_specs=P(("rep", "exp"), None),
        check_vma=False,
    )
```

```python
import jax
import jax.numpy as jnp
from jax import lax
from jax.experimental import pallas as pl
from jax.sharding import PartitionSpec as P

CAP = 72


def expert_block(x_ref, gate_ref, up_ref, down_ref, out_ref):
    x = x_ref[...]
    gate_value = jnp.dot(x, gate_ref[...], preferred_element_type=jnp.float32)
    up_value = jnp.dot(x, up_ref[...], preferred_element_type=jnp.float32)
    hidden = (gate_value / (1.0 + jnp.exp(-gate_value)) * up_value).astype(jnp.bfloat16)
    result = lax.dot_general(
        hidden, down_ref[...], (((1,), (1,)), ((), ())), preferred_element_type=jnp.float32
    )
    out_ref[...] = result.astype(out_ref.dtype)


def apply_experts(received, weights):
    sources, local_count, capacity, model_width = received.shape
    hidden_width = weights.shape[-1]
    row_block = received[:, 0].reshape(-1, model_width)
    rows = row_block.shape[0]
    block = 384
    def pick(k):
        return pl.BlockSpec((None, None, model_width, hidden_width), lambda i: (k, 0, 0, 0))
    result = pl.pallas_call(
        expert_block,
        grid=(rows // block,),
        in_specs=[pl.BlockSpec((block, model_width), lambda i: (i, 0)), pick(0), pick(1), pick(2)],
        out_specs=pl.BlockSpec((block, model_width), lambda i: (i, 0)),
        out_shape=jax.ShapeDtypeStruct((rows, model_width), jnp.bfloat16),
    )(row_block, weights, weights, weights)
    results = [result.reshape(sources, capacity, model_width)]
    return jnp.stack(results, axis=1)


def on_device(tokens, expert_ids, route_weights, placement_map, w_gate, w_up, down_rows):
    tok_rows, top_count = expert_ids.shape
    experts = placement_map.shape[0]
    local_experts = w_gate.shape[0]
    model_width = tokens.shape[1]
    groups = lax.axis_size("exp")
    slots_total = experts * CAP
    expert_range = jnp.arange(experts, dtype=jnp.int32)
    slot_ids = jnp.sum(jnp.where(expert_ids[:, :, None] == expert_range, placement_map, 0), axis=2)
    slot_hot = slot_ids[:, :, None] == expert_range
    token_hot = jnp.sum(slot_hot.astype(jnp.float32), axis=1).astype(jnp.bfloat16)
    row_range = jnp.arange(tok_rows, dtype=jnp.int32)
    earlier = (row_range[None, :] < row_range[:, None]).astype(jnp.bfloat16)
    before = jnp.dot(earlier, token_hot, preferred_element_type=jnp.float32)
    position = jnp.sum(jnp.where(slot_hot, before[:, None, :], 0.0), axis=2).astype(jnp.int32)
    target = slot_ids * CAP + position
    slot_range = jnp.arange(slots_total, dtype=jnp.int32)
    hits = target.T[:, :, None] == slot_range
    scatter = jnp.sum(hits.astype(jnp.float32), axis=0).astype(jnp.bfloat16)
    outgoing = lax.dot_general(
        scatter, tokens, (((0,), (0,)), ((), ())), preferred_element_type=jnp.float32
    ).astype(jnp.bfloat16)
    outgoing = outgoing.reshape(groups, local_experts, CAP, model_width)
    stacked = jnp.stack([w_gate, w_up, down_rows])
    stacked = lax.all_gather(stacked, "rep", axis=2, tiled=True)
    received = lax.all_to_all(outgoing, "exp", split_axis=0, concat_axis=0, tiled=True)
    returned = lax.all_to_all(
        apply_experts(received, stacked), "exp", split_axis=0, concat_axis=0, tiled=True
    )
    returned = returned.reshape(slots_total, model_width)
    combine = jnp.sum(jnp.where(hits, route_weights.T[:, :, None], 0.0), axis=0)
    combine_hi = combine.astype(jnp.bfloat16)
    combine_lo = (combine - combine_hi.astype(jnp.float32)).astype(jnp.bfloat16)
    mixed = jnp.dot(combine_hi, returned, preferred_element_type=jnp.float32)
    mixed = mixed + jnp.dot(combine_lo, returned, preferred_element_type=jnp.float32)
    return mixed.astype(jnp.bfloat16)


def solution(mesh):
    return jax.shard_map(
        on_device,
        mesh=mesh,
        in_specs=(
            P(("rep", "exp"), None),
            P(("rep", "exp"), None),
            P(("rep", "exp"), None),
            P(),
            P("exp", "rep", None),
            P("exp", "rep", None),
            P("exp", "rep", None),
        ),
        out_specs=P(("rep", "exp"), None),
        check_vma=False,
    )
```

```python
import jax
import jax.numpy as jnp
from jax import lax
from jax.experimental import pallas as pl
from jax.sharding import PartitionSpec as P

CAP = 72


def expert_block(x_ref, gate_ref, up_ref, down_ref, out_ref):
    x = x_ref[...]
    gate_value = jnp.dot(x, gate_ref[...], preferred_element_type=jnp.float32)
    up_value = jnp.dot(x, up_ref[...], preferred_element_type=jnp.float32)
    hidden = (gate_value / (1.0 + jnp.exp(-gate_value)) * up_value).astype(jnp.bfloat16)
    result = lax.dot_general(
        hidden, down_ref[...], (((1,), (1,)), ((), ())), preferred_element_type=jnp.float32
    )
    out_ref[...] = result.astype(out_ref.dtype)


def apply_experts(received, weights):
    sources, local_count, capacity, model_width = received.shape
    hidden_width = weights.shape[-1]
    row_block = received[:, 0].reshape(-1, model_width)
    rows = row_block.shape[0]
    block = 576
    def pick(k):
        return pl.BlockSpec((None, None, model_width, hidden_width), lambda i: (k, 0, 0, 0))
    result = pl.pallas_call(
        expert_block,
        grid=(rows // block,),
        in_specs=[pl.BlockSpec((block, model_width), lambda i: (i, 0)), pick(0), pick(1), pick(2)],
        out_specs=pl.BlockSpec((block, model_width), lambda i: (i, 0)),
        out_shape=jax.ShapeDtypeStruct((rows, model_width), jnp.bfloat16),
    )(row_block, weights, weights, weights)
    results = [result.reshape(sources, capacity, model_width)]
    return jnp.stack(results, axis=1)


def on_device(tokens, expert_ids, route_weights, placement_map, w_gate, w_up, down_rows):
    tok_rows, top_count = expert_ids.shape
    experts = placement_map.shape[0]
    local_experts = w_gate.shape[0]
    model_width = tokens.shape[1]
    groups = lax.axis_size("exp")
    slots_total = experts * CAP
    expert_range = jnp.arange(experts, dtype=jnp.int32)
    slot_ids = jnp.sum(jnp.where(expert_ids[:, :, None] == expert_range, placement_map, 0), axis=2)
    slot_hot = slot_ids[:, :, None] == expert_range
    token_hot = jnp.sum(slot_hot.astype(jnp.float32), axis=1).astype(jnp.bfloat16)
    row_range = jnp.arange(tok_rows, dtype=jnp.int32)
    earlier = (row_range[None, :] < row_range[:, None]).astype(jnp.bfloat16)
    before = jnp.dot(earlier, token_hot, preferred_element_type=jnp.float32)
    position = jnp.sum(jnp.where(slot_hot, before[:, None, :], 0.0), axis=2).astype(jnp.int32)
    target = slot_ids * CAP + position
    slot_range = jnp.arange(slots_total, dtype=jnp.int32)
    hits = target.T[:, :, None] == slot_range
    scatter = jnp.sum(hits.astype(jnp.float32), axis=0).astype(jnp.bfloat16)
    outgoing = lax.dot_general(
        scatter, tokens, (((0,), (0,)), ((), ())), preferred_element_type=jnp.float32
    ).astype(jnp.bfloat16)
    outgoing = outgoing.reshape(groups, local_experts, CAP, model_width)
    stacked = jnp.stack([w_gate, w_up, down_rows])
    stacked = lax.all_gather(stacked, "rep", axis=2, tiled=True)
    received = lax.all_to_all(outgoing, "exp", split_axis=0, concat_axis=0, tiled=True)
    returned = lax.all_to_all(
        apply_experts(received, stacked), "exp", split_axis=0, concat_axis=0, tiled=True
    )
    returned = returned.reshape(slots_total, model_width)
    combine = jnp.sum(jnp.where(hits, route_weights.T[:, :, None], 0.0), axis=0)
    combine_hi = combine.astype(jnp.bfloat16)
    combine_lo = (combine - combine_hi.astype(jnp.float32)).astype(jnp.bfloat16)
    mixed = jnp.dot(combine_hi, returned, preferred_element_type=jnp.float32)
    mixed = mixed + jnp.dot(combine_lo, returned, preferred_element_type=jnp.float32)
    return mixed.astype(jnp.bfloat16)


def solution(mesh):
    return jax.shard_map(
        on_device,
        mesh=mesh,
        in_specs=(
            P(("rep", "exp"), None),
            P(("rep", "exp"), None),
            P(("rep", "exp"), None),
            P(),
            P("exp", "rep", None),
            P("exp", "rep", None),
            P("exp", "rep", None),
        ),
        out_specs=P(("rep", "exp"), None),
        check_vma=False,
    )
```

```python
import jax
import jax.numpy as jnp
from jax import lax
from jax.experimental import pallas as pl
from jax.sharding import PartitionSpec as P

CAP = 72


def expert_block(x_ref, gate_up_ref, down_ref, out_ref):
    x = x_ref[...]
    hidden_width = down_ref.shape[-1]
    both = jnp.dot(x, gate_up_ref[...], preferred_element_type=jnp.float32)
    gate_value, up_value = both[:, :hidden_width], both[:, hidden_width:]
    hidden = (gate_value / (1.0 + jnp.exp(-gate_value)) * up_value).astype(jnp.bfloat16)
    result = lax.dot_general(
        hidden, down_ref[...], (((1,), (1,)), ((), ())), preferred_element_type=jnp.float32
    )
    out_ref[...] = result.astype(out_ref.dtype)


def apply_experts(received, weights, hidden_width):
    sources, local_count, capacity, model_width = received.shape
    row_block = received[:, 0].reshape(-1, model_width)
    rows = row_block.shape[0]
    block = 384
    result = pl.pallas_call(
        expert_block,
        grid=(rows // block,),
        in_specs=[
            pl.BlockSpec((block, model_width), lambda i: (i, 0)),
            pl.BlockSpec((None, model_width, 2 * hidden_width), lambda i: (0, 0, 0)),
            pl.BlockSpec((None, model_width, hidden_width), lambda i: (0, 0, 2)),
        ],
        out_specs=pl.BlockSpec((block, model_width), lambda i: (i, 0)),
        out_shape=jax.ShapeDtypeStruct((rows, model_width), jnp.bfloat16),
    )(row_block, weights, weights)
    results = [result.reshape(sources, capacity, model_width)]
    return jnp.stack(results, axis=1)


def on_device(tokens, expert_ids, route_weights, placement_map, w_gate, w_up, down_rows):
    tok_rows, top_count = expert_ids.shape
    experts = placement_map.shape[0]
    local_experts = w_gate.shape[0]
    model_width = tokens.shape[1]
    groups = lax.axis_size("exp")
    slots_total = experts * CAP
    expert_range = jnp.arange(experts, dtype=jnp.int32)
    slot_ids = jnp.sum(jnp.where(expert_ids[:, :, None] == expert_range, placement_map, 0), axis=2)
    slot_hot = slot_ids[:, :, None] == expert_range
    token_hot = jnp.sum(slot_hot.astype(jnp.float32), axis=1).astype(jnp.bfloat16)
    row_range = jnp.arange(tok_rows, dtype=jnp.int32)
    earlier = (row_range[None, :] < row_range[:, None]).astype(jnp.bfloat16)
    before = jnp.dot(earlier, token_hot, preferred_element_type=jnp.float32)
    position = jnp.sum(jnp.where(slot_hot, before[:, None, :], 0.0), axis=2).astype(jnp.int32)
    target = slot_ids * CAP + position
    slot_range = jnp.arange(slots_total, dtype=jnp.int32)
    hits = target.T[:, :, None] == slot_range
    scatter = jnp.sum(hits.astype(jnp.float32), axis=0).astype(jnp.bfloat16)
    outgoing = lax.dot_general(
        scatter, tokens, (((0,), (0,)), ((), ())), preferred_element_type=jnp.float32
    ).astype(jnp.bfloat16)
    outgoing = outgoing.reshape(groups, local_experts, CAP, model_width)
    stacked = jnp.concatenate([w_gate, w_up, down_rows], axis=2)
    stacked = lax.all_gather(stacked, "rep", axis=1, tiled=True)
    received = lax.all_to_all(outgoing, "exp", split_axis=0, concat_axis=0, tiled=True)
    returned = lax.all_to_all(
        apply_experts(received, stacked, w_gate.shape[2]), "exp", split_axis=0, concat_axis=0, tiled=True
    )
    returned = returned.reshape(slots_total, model_width)
    combine = jnp.sum(jnp.where(hits, route_weights.T[:, :, None], 0.0), axis=0)
    combine_hi = combine.astype(jnp.bfloat16)
    combine_lo = (combine - combine_hi.astype(jnp.float32)).astype(jnp.bfloat16)
    mixed = jnp.dot(combine_hi, returned, preferred_element_type=jnp.float32)
    mixed = mixed + jnp.dot(combine_lo, returned, preferred_element_type=jnp.float32)
    return mixed.astype(jnp.bfloat16)


def solution(mesh):
    return jax.shard_map(
        on_device,
        mesh=mesh,
        in_specs=(
            P(("rep", "exp"), None),
            P(("rep", "exp"), None),
            P(("rep", "exp"), None),
            P(),
            P("exp", "rep", None),
            P("exp", "rep", None),
            P("exp", "rep", None),
        ),
        out_specs=P(("rep", "exp"), None),
        check_vma=False,
    )
```

```python
import jax
import jax.numpy as jnp
import numpy as np
from jax import lax
from jax.sharding import PartitionSpec as P

CAP = 72


def apply_experts(received, weights):
    sources, local_count, capacity, model_width = received.shape
    row_block = received[:, 0].reshape(-1, model_width)
    gate_value = jnp.dot(row_block, weights[0, 0], preferred_element_type=jnp.float32)
    up_value = jnp.dot(row_block, weights[1, 0], preferred_element_type=jnp.float32)
    hidden = (jax.nn.silu(gate_value) * up_value).astype(jnp.bfloat16)
    hidden = lax.optimization_barrier(hidden)
    result = lax.dot_general(
        hidden, weights[2, 0], (((1,), (1,)), ((), ())), preferred_element_type=jnp.float32
    )
    results = [result.astype(jnp.bfloat16).reshape(sources, capacity, model_width)]
    return jnp.stack(results, axis=1)


def on_device(tokens, expert_ids, route_weights, placement_map, w_gate, w_up, down_rows):
    tok_rows, top_count = expert_ids.shape
    experts = placement_map.shape[0]
    local_experts = w_gate.shape[0]
    model_width = tokens.shape[1]
    groups = lax.axis_size("exp")
    slots_total = experts * CAP
    expert_range = jnp.arange(experts, dtype=jnp.int32)
    holder = jnp.sum(jnp.where(placement_map[:, None] == expert_range, expert_range[:, None], 0), axis=0)
    slot_hot = expert_ids[:, :, None] == holder
    token_hot = jnp.sum(slot_hot.astype(jnp.float32), axis=1).astype(jnp.bfloat16)
    row_range = jnp.arange(tok_rows, dtype=jnp.int32)
    earlier = (row_range[None, :] < row_range[:, None]).astype(jnp.bfloat16)
    before = jnp.dot(earlier, token_hot, preferred_element_type=jnp.float32)
    slot_base = np.arange(experts, dtype=np.float32) * CAP
    target = jnp.sum(jnp.where(slot_hot, before[:, None, :] + slot_base, 0.0), axis=2).astype(jnp.int32)
    slot_range = jnp.arange(slots_total, dtype=jnp.int32)
    hits = target.T[:, :, None] == slot_range
    scatter = jnp.sum(hits.astype(jnp.float32), axis=0).astype(jnp.bfloat16)
    outgoing = lax.dot_general(
        scatter, tokens, (((0,), (0,)), ((), ())), preferred_element_type=jnp.float32
    ).astype(jnp.bfloat16)
    outgoing = outgoing.reshape(groups, local_experts, CAP, model_width)
    stacked = jnp.stack([w_gate, w_up, down_rows])
    stacked = lax.all_gather(stacked, "rep", axis=2, tiled=True)
    received = lax.all_to_all(outgoing, "exp", split_axis=0, concat_axis=0, tiled=True)
    returned = lax.all_to_all(
        apply_experts(received, stacked), "exp", split_axis=0, concat_axis=0, tiled=True
    )
    returned = returned.reshape(slots_total, model_width)
    combine = jnp.sum(jnp.where(hits, route_weights.T[:, :, None], 0.0), axis=0)
    combine_hi = combine.astype(jnp.bfloat16)
    combine_lo = (combine - combine_hi.astype(jnp.float32)).astype(jnp.bfloat16)
    mixed = jnp.dot(combine_hi, returned, preferred_element_type=jnp.float32)
    mixed = mixed + jnp.dot(combine_lo, returned, preferred_element_type=jnp.float32)
    return mixed.astype(jnp.bfloat16)


def solution(mesh):
    return jax.shard_map(
        on_device,
        mesh=mesh,
        in_specs=(
            P(("rep", "exp"), None),
            P(("rep", "exp"), None),
            P(("rep", "exp"), None),
            P(),
            P("exp", "rep", None),
            P("exp", "rep", None),
            P("exp", "rep", None),
        ),
        out_specs=P(("rep", "exp"), None),
        check_vma=False,
    )
```
